256 devices in a mesh: pipe: 16 (over z, core), seq: 16 (over y, x).
Axes of the slice: x: 4, y: 4, z: 8, core: 2. Of those that a mesh axis runs over, the one named last changes fastest.
Arguments:
- queries: bfloat16 [16, 1024, 4096], P('pipe', 'seq'), may hold values from -6 to 6
- keys: bfloat16 [16, 1024, 4096], P('pipe', 'seq'), may hold values from -6 to 6
- values: bfloat16 [16, 1024, 4096], P('pipe', 'seq'), may hold values from -6 to 6
- out_weight: bfloat16 [16, 4096, 5120], P('pipe', None, 'seq'), may hold values from -0.375 to 0.375
- head_class: int32 [16, 32], P('pipe'), may hold values from 0 to 1
- kv_blocks: int32 [16, 32, 16, 16], P('pipe'), may hold values from 0 to 15, as said below
- kv_count: int32 [16, 32], P('pipe'), may hold values from 1 to 16, as said below
Outputs:
- handed: bfloat16 [16, 1024, 5120], P('pipe', 'seq')
The draws below stay inside these ranges and needn't reach their ends.
Inputs may be any that keep to these rules, and one draw needn't show every extreme that they name: `kv_blocks`: in every row the entries are distinct, and the first is the query block itself. `kv_count`: in every section some head uses all 16 entries.
All inputs are finite; a program needn't handle non-finite values.
Results may differ from the reference program's by a relative error of at most 0.018.
Values may be sent and summed in bfloat16 or wider, within the bound.
No kernel may reach another device: no remote copies, remote signals or barrier semaphores. Data moves between devices by JAX's collectives and lax.ppermute only.
A program may use at most 64 MiB of HBM per device.

```python
import jax
import jax.numpy as jnp
from jax import lax

HEAD_SIZE = 128
DM = 5120
FRAMES = 4
BLOCK = 64
LIVE = 16
SEGMENTS = 16
HEADS = 32
TOKENS = 1024
POS = 256
NB = 16


def query_key_pair(key):
    row_width = HEADS * HEAD_SIZE
    shape_all = (SEGMENTS, TOKENS, row_width)
    query_all = jnp.clip(jax.random.normal(jax.random.fold_in(key, 11), shape_all, jnp.float32), -6.0, 6.0)
    key_all = jnp.clip(jax.random.normal(jax.random.fold_in(key, 12), shape_all, jnp.float32), -6.0, 6.0)
    return (query_all.astype(jnp.bfloat16), key_all.astype(jnp.bfloat16))


def draw_queries(key, part):
    return query_key_pair(key)[0]


def draw_keys(key, part):
    return query_key_pair(key)[1]


def draw_kv_blocks(key, part):
    raw_draw = jax.random.randint(key, (SEGMENTS, HEADS, NB, NB), 0, 2 ** 20, dtype=jnp.int32)
    columns = jnp.arange(NB, dtype=jnp.int32)
    logit_scores = raw_draw * NB + columns[None, None, None, :]
    own_block = columns[:, None] == columns[None, :]
    logit_scores = jnp.where(own_block[None, None, :, :], 2 ** 30, logit_scores)
    unused, chosen = lax.top_k(logit_scores, LIVE)
    return chosen.astype(jnp.int32)


def draw_kv_count(key, part):
    raw_draw = jax.random.randint(jax.random.fold_in(key, 1), (SEGMENTS, HEADS), 0, LIVE, dtype=jnp.int32)
    counts = 1 + raw_draw * raw_draw * raw_draw // (LIVE * LIVE)
    heavy_head = jax.random.randint(jax.random.fold_in(key, 2), (SEGMENTS, 1), 0, HEADS, dtype=jnp.int32)
    head_ids = jnp.arange(HEADS, dtype=jnp.int32)[None, :]
    return jnp.where(head_ids == heavy_head, LIVE, counts).astype(jnp.int32)


def with_ends(entries, key, smallest, top_value):
    shape = entries.shape
    place = [jax.random.randint(jax.random.fold_in(key, axis), (), 0, shape[axis]) for axis in range(len(shape))]
    entries = entries.at[tuple(place)].set(smallest)
    longest = shape.index(max(shape))
    place[longest] = (place[longest] + 1) % shape[longest]
    return entries.at[tuple(place)].set(top_value)


def steps_of(stream_key, dims, cuts, low, top_value):
    level = 1.0
    for dim, parts in cuts:
        heights = jax.random.uniform(jax.random.fold_in(jax.random.fold_in(stream_key, 6), dim), (parts,), jnp.float32, low / len(cuts), top_value / len(cuts))
        level = level * jnp.repeat(jnp.exp(heights), dims[dim] // parts).reshape((-1,) + (1,) * (len(dims) - 1 - dim))
    return level


def bell_draw(own_key, dims, deviation, limit, split=(), held_as=jnp.bfloat16):
    level = steps_of(own_key, dims, split, -0.22, 0.18) if split else 1.0
    values = jax.random.normal(own_key, dims, jnp.float32) * deviation * level
    return jnp.minimum(jnp.maximum(values, -limit), limit).astype(held_as)


def setup_inputs(seed: int = 0) -> dict:
    streams_of = jax.random.split(jax.random.key(seed), 8)
    queries = draw_queries(jax.random.fold_in(streams_of[7], 71), 0)
    keys = draw_keys(jax.random.fold_in(streams_of[7], 71), 0)
    values = bell_draw(streams_of[2], (SEGMENTS, TOKENS, HEADS * HEAD_SIZE), 1.0, 6.0, ((0, 16), (1, 16)))
    out_weight = bell_draw(streams_of[3], (SEGMENTS, HEADS * HEAD_SIZE, DM), (HEADS * HEAD_SIZE // 16) ** -0.5, 0.375, ((0, 16), (2, 16)))
    head_class = with_ends(jax.random.randint(streams_of[4], (SEGMENTS, HEADS), 0, 2), jax.random.fold_in(streams_of[4], 1), 0, 1).astype(jnp.int32)
    kv_blocks = draw_kv_blocks(jax.random.fold_in(streams_of[7], 71), 0)
    kv_count = draw_kv_count(jax.random.fold_in(streams_of[7], 71), 0)
    return {"queries": queries, "keys": keys, "values": values, "out_weight": out_weight, "head_class": head_class, "kv_blocks": kv_blocks, "kv_count": kv_count}


def frame_to_pos(tensor):
    return tensor.reshape(FRAMES, POS, -1).transpose(1, 0, 2).reshape(TOKENS, -1)


def pos_to_frame(tensor):
    return tensor.reshape(POS, FRAMES, -1).transpose(1, 0, 2).reshape(TOKENS, -1)


def one_head(inputs):
    query_rows, key_rows, value_rows, head_kind, blocks, live_count = inputs
    temporal = head_kind == 1
    query_rows = jnp.where(temporal, frame_to_pos(query_rows), query_rows)
    key_rows = jnp.where(temporal, frame_to_pos(key_rows), key_rows)
    value_rows = jnp.where(temporal, frame_to_pos(value_rows), value_rows)
    query_tiles = query_rows.reshape(NB, BLOCK, HEAD_SIZE).astype(jnp.float32)
    key_blocks = key_rows.reshape(NB, BLOCK, HEAD_SIZE)
    value_blocks = value_rows.reshape(NB, BLOCK, HEAD_SIZE)
    selected_keys = key_blocks[blocks].reshape(NB, LIVE * BLOCK, HEAD_SIZE).astype(jnp.float32)
    selected_values = value_blocks[blocks].reshape(NB, LIVE * BLOCK, HEAD_SIZE).astype(jnp.float32)
    logit_scores = jnp.einsum("ure,ute->urt", query_tiles, selected_keys) * (HEAD_SIZE ** -0.5)
    live_mask = jnp.repeat(jnp.arange(LIVE) < live_count, BLOCK)[None, None, :]
    logit_scores = jnp.where(live_mask, logit_scores, -jnp.inf)
    row_max = jnp.max(logit_scores, axis=-1, keepdims=True)
    probs = jnp.where(live_mask, jnp.exp(logit_scores - row_max), 0.0)
    softmax_denominator = jnp.sum(probs, axis=-1, keepdims=True)
    block_probabilities = probs.astype(jnp.bfloat16)
    attended_values = jnp.einsum("yhn,yng->yhg", block_probabilities.astype(jnp.float32), selected_values) / softmax_denominator
    attended_values = attended_values.reshape(TOKENS, HEAD_SIZE)
    attended_values = jnp.where(temporal, pos_to_frame(attended_values), attended_values)
    return attended_values.astype(jnp.bfloat16)


def one_segment(inputs):
    query_rows, key_rows, value_rows, weight, classes, blocks, counts = inputs
    def split_heads(tensor):
        return tensor.reshape(TOKENS, HEADS, HEAD_SIZE).transpose(1, 0, 2)
    result = lax.map(one_head, (split_heads(query_rows), split_heads(key_rows), split_heads(value_rows), classes, blocks, counts))
    attended_values = result.transpose(1, 0, 2).reshape(TOKENS, HEADS * HEAD_SIZE)
    return jnp.dot(attended_values, weight, preferred_element_type=jnp.float32).astype(jnp.bfloat16)


def reference(queries, keys, values, out_weight, head_class, kv_blocks, kv_count):
    projected = lax.map(one_segment, (queries, keys, values, out_weight, head_class, kv_blocks, kv_count))
    return jnp.roll(projected, 1, axis=0)
```

```python
import jax
import jax.numpy as jnp
from jax import lax
from jax.sharding import Mesh, PartitionSpec as P

FRAMES = 4
BLOCK = 64


def from_behind(value, axis, steps):
    count = lax.axis_size(axis)
    pairs = [(source, (source + steps) % count) for source in range(count)]
    return lax.ppermute(value, axis, pairs)


def frame_to_pos(tensor):
    token_total, row_width = tensor.shape
    return (
        tensor.reshape(FRAMES, token_total // FRAMES, row_width)
        .transpose(1, 0, 2)
        .reshape(token_total, row_width)
    )


def pos_to_frame(tensor):
    token_total, row_width = tensor.shape
    return (
        tensor.reshape(token_total // FRAMES, FRAMES, row_width)
        .transpose(1, 0, 2)
        .reshape(token_total, row_width)
    )


def attend_head(query_rows, key_rows, value_rows, temporal, blocks, live_count):
    token_total, head_width = query_rows.shape
    nblock = token_total // BLOCK
    query_rows, key_rows, value_rows = lax.cond(
        temporal,
        lambda tensors: tuple((frame_to_pos(tensor) for tensor in tensors)),
        lambda tensors: tensors,
        (query_rows, key_rows, value_rows),
    )
    query_tiles = query_rows.reshape(nblock, BLOCK, head_width)
    key_blocks = key_rows.reshape(nblock, BLOCK, head_width)
    value_blocks = value_rows.reshape(nblock, BLOCK, head_width)
    score_scale = head_width ** (-0.5)
    columns = jnp.arange(2 * BLOCK)

    def advance(pair_index, state_now):
        running_max, weight_sum, numerator = state_now
        chosen = lax.dynamic_slice_in_dim(blocks, 2 * pair_index, 2, 1)
        selected_keys = key_blocks[chosen].reshape(nblock, 2 * BLOCK, head_width)
        selected_values = value_blocks[chosen].reshape(nblock, 2 * BLOCK, head_width)
        logit_scores = (
            jnp.einsum(
                "ure,ute->urt", query_tiles, selected_keys, preferred_element_type=jnp.float32
            )
            * score_scale
        )
        usable = (columns < BLOCK) | (2 * pair_index + 1 < live_count)
        logit_scores = jnp.where(usable[None, None, :], logit_scores, -jnp.inf)
        newest_max = jnp.maximum(running_max, jnp.max(logit_scores, axis=-1))
        weights_now = jnp.exp(logit_scores - newest_max[..., None])
        factor = jnp.exp(running_max - newest_max)
        weight_sum = weight_sum * factor + jnp.sum(weights_now, axis=-1)
        numerator = numerator * factor[..., None] + jnp.einsum(
            "yhn,yng->yhg",
            weights_now.astype(jnp.bfloat16),
            selected_values,
            preferred_element_type=jnp.float32,
        )
        return (newest_max, weight_sum, numerator)

    initial = (
        jnp.full((nblock, BLOCK), -jnp.inf, jnp.float32),
        jnp.zeros((nblock, BLOCK), jnp.float32),
        jnp.zeros((nblock, BLOCK, head_width), jnp.float32),
    )
    running_max, weight_sum, numerator = lax.fori_loop(0, (live_count + 1) // 2, advance, initial)
    result = (numerator / weight_sum[..., None]).reshape(token_total, head_width)
    result = lax.cond(temporal, pos_to_frame, lambda tensor: tensor, result)
    return result.astype(jnp.bfloat16)


def shards(queries, keys, values, out_weight, head_class, kv_blocks, kv_count):
    rows_n = lax.axis_size("sy")
    cols_n = lax.axis_size("sx")
    members = rows_n * cols_n
    head_total = head_class.shape[1]
    per_dev = head_total // members
    head_width = queries.shape[2] // head_total
    classes = head_class[0]
    blocks = kv_blocks[0]
    counts = kv_count[0]
    query_rows = queries[0]
    key_rows = keys[0]
    value_rows = values[0]
    weight_local = out_weight[0]
    token_total = query_rows.shape[0] * members
    width_local = weight_local.shape[1]
    placing = jnp.arange(head_total, dtype=jnp.int32)
    weight_mine = lax.all_to_all(weight_local, "sy", split_axis=0, concat_axis=1, tiled=True)
    exchanged = (
        lax.all_to_all(query_rows, ("sy", "sx"), split_axis=1, concat_axis=0, tiled=True),
        lax.all_to_all(key_rows, ("sy", "sx"), split_axis=1, concat_axis=0, tiled=True),
        lax.all_to_all(value_rows, ("sy", "sx"), split_axis=1, concat_axis=0, tiled=True),
    )
    place = lax.axis_index("sy") * cols_n + lax.axis_index("sx")
    own_heads = lax.dynamic_slice_in_dim(placing, place * per_dev, per_dev)
    results = []
    for slot in range(per_dev):
        head_now = own_heads[slot]
        lo_col = slot * head_width
        hi_col = lo_col + head_width
        results.append(
            attend_head(
                exchanged[0][:, lo_col:hi_col],
                exchanged[1][:, lo_col:hi_col],
                exchanged[2][:, lo_col:hi_col],
                classes[head_now] == 1,
                blocks[head_now],
                counts[head_now],
            )
        )
    joined = jnp.concatenate(results, axis=1)
    gathered = lax.all_gather(joined, "sx", axis=1, tiled=True)
    partial = jnp.dot(gathered, weight_mine, preferred_element_type=jnp.float32).astype(jnp.bfloat16)
    reduced = lax.psum_scatter(partial, "sy", scatter_dimension=0, tiled=True)
    spread = lax.all_to_all(reduced, "sx", split_axis=0, concat_axis=1, tiled=True)
    rows_here = spread.shape[0]
    projected = (
        spread.reshape(rows_here, cols_n, rows_n, width_local)
        .transpose(0, 2, 1, 3)
        .reshape(rows_here, cols_n * rows_n * width_local)
    )
    handed = from_behind(projected, "pipe", 1)
    return handed[None]


def solution(mesh):
    pipe_n, seq_n = mesh.devices.shape
    side = int(round(seq_n ** 0.5))
    grid = Mesh(mesh.devices.reshape(pipe_n, seq_n // side, side), ("pipe", "sy", "sx"))
    seq = ("sy", "sx")
    placed = (
        P("pipe", seq, None),
        P("pipe", seq, None),
        P("pipe", seq, None),
        P("pipe", None, seq),
        P("pipe", None),
        P("pipe", None, None, None),
        P("pipe", None),
    )
    return jax.shard_map(
        shards, mesh=grid, in_specs=placed, out_specs=P("pipe", seq, None), check_vma=False
    )
```

```python
import jax
import jax.numpy as jnp
from jax import lax
from jax.sharding import Mesh, PartitionSpec as P

FRAMES = 4
BLOCK = 64


def from_behind(value, axis, steps):
    count = lax.axis_size(axis)
    pairs = [(source, (source + steps) % count) for source in range(count)]
    return lax.ppermute(value, axis, pairs)


def frame_to_pos(tensor):
    token_total, row_width = tensor.shape
    return (
        tensor.reshape(FRAMES, token_total // FRAMES, row_width)
        .transpose(1, 0, 2)
        .reshape(token_total, row_width)
    )


def pos_to_frame(tensor):
    token_total, row_width = tensor.shape
    return (
        tensor.reshape(token_total // FRAMES, FRAMES, row_width)
        .transpose(1, 0, 2)
        .reshape(token_total, row_width)
    )


def attend_head(query_rows, key_rows, value_rows, temporal, blocks, live_count):
    token_total, head_width = query_rows.shape
    nblock = token_total // BLOCK
    query_rows, key_rows, value_rows = lax.cond(
        temporal,
        lambda tensors: tuple((frame_to_pos(tensor) for tensor in tensors)),
        lambda tensors: tensors,
        (query_rows, key_rows, value_rows),
    )
    query_tiles = query_rows.reshape(nblock, BLOCK, head_width)
    key_blocks = key_rows.reshape(nblock, BLOCK, head_width)
    value_blocks = value_rows.reshape(nblock, BLOCK, head_width)
    score_scale = head_width ** (-0.5)
    columns = jnp.arange(2 * BLOCK)

    def advance(pair_index, state_now):
        running_max, weight_sum, numerator = state_now
        chosen = lax.dynamic_slice_in_dim(blocks, 2 * pair_index, 2, 1)
        selected_keys = key_blocks[chosen].reshape(nblock, 2 * BLOCK, head_width)
        selected_values = value_blocks[chosen].reshape(nblock, 2 * BLOCK, head_width)
        logit_scores = (
            jnp.einsum(
                "ure,ute->urt", query_tiles, selected_keys, preferred_element_type=jnp.float32
            )
            * score_scale
        )
        usable = (columns < BLOCK) | (2 * pair_index + 1 < live_count)
        logit_scores = jnp.where(usable[None, None, :], logit_scores, -jnp.inf)
        newest_max = jnp.maximum(running_max, jnp.max(logit_scores, axis=-1))
        weights_now = jnp.exp(logit_scores - newest_max[..., None])
        factor = jnp.exp(running_max - newest_max)
        weight_sum = weight_sum * factor + jnp.sum(weights_now, axis=-1)
        numerator = numerator * factor[..., None] + jnp.einsum(
            "yhn,yng->yhg",
            weights_now.astype(jnp.bfloat16),
            selected_values,
            preferred_element_type=jnp.float32,
        )
        return (newest_max, weight_sum, numerator)

    initial = (
        jnp.full((nblock, BLOCK), -jnp.inf, jnp.float32),
        jnp.zeros((nblock, BLOCK), jnp.float32),
        jnp.zeros((nblock, BLOCK, head_width), jnp.float32),
    )
    running_max, weight_sum, numerator = lax.fori_loop(0, (live_count + 1) // 2, advance, initial)
    result = (numerator / weight_sum[..., None]).reshape(token_total, head_width)
    result = lax.cond(temporal, pos_to_frame, lambda tensor: tensor, result)
    return result.astype(jnp.bfloat16)


def shifted(value, axis, steps):
    count = lax.axis_size(axis)
    if steps % count == 0:
        return value
    pairs = [(source, (source + steps) % count) for source in range(count)]
    return lax.ppermute(value, axis, pairs)


def canonical(pieces, here):
    count = len(pieces)
    order = (here - jnp.arange(count)) % count
    return jnp.stack(pieces)[order]


def shards(queries, keys, values, out_weight, head_class, kv_blocks, kv_count):
    rows_n = lax.axis_size("sy")
    cols_n = lax.axis_size("sx")
    pipe_n = lax.axis_size("pipe")
    members = rows_n * cols_n
    head_total = head_class.shape[1]
    per_dev = head_total // members
    head_width = queries.shape[2] // head_total
    classes = head_class[0]
    blocks = kv_blocks[0]
    counts = kv_count[0]
    weight_local = out_weight[0]
    in_total, width_local = weight_local.shape
    in_rows = in_total // rows_n
    row_here = lax.axis_index("sy")
    col_here = lax.axis_index("sx")

    weight_pieces = [
        shifted(
            lax.dynamic_slice_in_dim(weight_local, ((row_here + step) % rows_n) * in_rows, in_rows, 0),
            "sy",
            step,
        )
        for step in range(rows_n)
    ]
    weight_mine = canonical(weight_pieces, row_here)

    stacked = jnp.stack([queries[0], keys[0], values[0]], axis=1)
    exchanged = lax.all_to_all(stacked, ("sy", "sx"), split_axis=2, concat_axis=0, tiled=True)
    place = row_here * cols_n + col_here
    own_heads = place * per_dev + jnp.arange(per_dev, dtype=jnp.int32)
    results = []
    for slot in range(per_dev):
        head_now = own_heads[slot]
        lo_col = slot * head_width
        hi_col = lo_col + head_width
        results.append(
            attend_head(
                exchanged[:, 0, lo_col:hi_col],
                exchanged[:, 1, lo_col:hi_col],
                exchanged[:, 2, lo_col:hi_col],
                classes[head_now] == 1,
                blocks[head_now],
                counts[head_now],
            )
        )
    joined = jnp.concatenate(results, axis=1)
    pair_rows = joined.shape[1]
    partial = None
    for step in range(cols_n):
        piece = shifted(joined, "sx", step)
        source = (col_here - step) % cols_n
        rows_w = lax.dynamic_slice_in_dim(weight_mine, source * pair_rows, pair_rows, 1)
        term = jnp.einsum(
            "te,kec->tkc", piece, rows_w, preferred_element_type=jnp.float32
        )
        partial = term if partial is None else partial + term
    token_total = partial.shape[0]
    chunk = token_total // rows_n
    partial = partial.reshape(token_total, rows_n * width_local).astype(jnp.bfloat16)
    reduced = None
    for step in range(rows_n):
        send = lax.dynamic_slice_in_dim(partial, ((row_here + step) % rows_n) * chunk, chunk, 0)
        got = shifted(send, "sy", step).astype(jnp.float32)
        reduced = got if reduced is None else reduced + got
    reduced = reduced.astype(jnp.bfloat16)
    rows_out = chunk // cols_n
    out_pieces = []
    for step in range(cols_n):
        send = lax.dynamic_slice_in_dim(reduced, ((col_here + step) % cols_n) * rows_out, rows_out, 0)
        pairs = [
            (p * cols_n + c, ((p + 1) % pipe_n) * cols_n + (c + step) % cols_n)
            for p in range(pipe_n)
            for c in range(cols_n)
        ]
        out_pieces.append(lax.ppermute(send, ("pipe", "sx"), pairs))
    ordered = canonical(out_pieces, col_here)
    handed = (
        ordered.reshape(cols_n, rows_out, rows_n, width_local)
        .transpose(1, 2, 0, 3)
        .reshape(rows_out, cols_n * rows_n * width_local)
    )
    return handed[None]


def solution(mesh):
    pipe_n, seq_n = mesh.devices.shape
    side = int(round(seq_n ** 0.5))
    grid = Mesh(mesh.devices.reshape(pipe_n, seq_n // side, side), ("pipe", "sy", "sx"))
    seq = ("sy", "sx")
    placed = (
        P("pipe", seq, None),
        P("pipe", seq, None),
        P("pipe", seq, None),
        P("pipe", None, seq),
        P("pipe", None),
        P("pipe", None, None, None),
        P("pipe", None),
    )
    return jax.shard_map(
        shards, mesh=grid, in_specs=placed, out_specs=P("pipe", seq, None), check_vma=False
    )
```

```python
import jax
import jax.numpy as jnp
from jax import lax
from jax.sharding import Mesh, PartitionSpec as P

FRAMES = 4
BLOCK = 64


def from_behind(value, axis, steps):
    count = lax.axis_size(axis)
    pairs = [(source, (source + steps) % count) for source in range(count)]
    return lax.ppermute(value, axis, pairs)


def frame_to_pos(tensor):
    token_total, row_width = tensor.shape
    return (
        tensor.reshape(FRAMES, token_total // FRAMES, row_width)
        .transpose(1, 0, 2)
        .reshape(token_total, row_width)
    )


def pos_to_frame(tensor):
    token_total, row_width = tensor.shape
    return (
        tensor.reshape(token_total // FRAMES, FRAMES, row_width)
        .transpose(1, 0, 2)
        .reshape(token_total, row_width)
    )


def block_of(temporal, token_total):
    tokens = jnp.arange(token_total, dtype=jnp.int32)
    per_frame = token_total // FRAMES
    spatial_block = tokens // BLOCK
    temporal_block = (tokens % per_frame) // (BLOCK // FRAMES)
    return jnp.where(temporal[:, None], temporal_block[None, :], spatial_block[None, :])


def attend_dense(query_rows, key_rows, value_rows, temporal, blocks, live_count):
    token_total, head_n, head_width = query_rows.shape
    nblock = token_total // BLOCK
    listed = jnp.arange(blocks.shape[-1], dtype=jnp.int32)
    live = listed[None, None, :] < live_count[:, None, None]
    chosen = (blocks[..., None] == jnp.arange(nblock, dtype=jnp.int32)) & live[..., None]
    allowed = jnp.any(chosen, axis=2).astype(jnp.bfloat16)
    owner = block_of(temporal, token_total)
    one_hot = (owner[..., None] == jnp.arange(nblock, dtype=jnp.int32)).astype(jnp.bfloat16)
    row_allowed = jnp.einsum("hqi,hib->hqb", one_hot, allowed, preferred_element_type=jnp.float32)
    keep = jnp.einsum(
        "hqb,hkb->hqk", row_allowed.astype(jnp.bfloat16), one_hot, preferred_element_type=jnp.float32
    )
    logit_scores = jnp.einsum(
        "qhd,khd->hqk", query_rows, key_rows, preferred_element_type=jnp.float32
    ) * (head_width ** (-0.5))
    logit_scores = jnp.where(keep > 0.5, logit_scores, -jnp.inf)
    row_max = jnp.max(logit_scores, axis=-1, keepdims=True)
    probs = jnp.exp(logit_scores - row_max)
    denom = jnp.sum(probs, axis=-1)
    weighted = jnp.einsum(
        "hqk,khd->qhd", probs.astype(jnp.bfloat16), value_rows, preferred_element_type=jnp.float32
    )
    result = weighted / jnp.transpose(denom)[..., None]
    return result.astype(jnp.bfloat16).reshape(token_total, head_n * head_width)


def shifted(value, axis, steps):
    count = lax.axis_size(axis)
    if steps % count == 0:
        return value
    pairs = [(source, (source + steps) % count) for source in range(count)]
    return lax.ppermute(value, axis, pairs)


def canonical(pieces, here):
    count = len(pieces)
    order = (here - jnp.arange(count)) % count
    return jnp.stack(pieces)[order]


def shards(queries, keys, values, out_weight, head_class, kv_blocks, kv_count):
    rows_n = lax.axis_size("sy")
    cols_n = lax.axis_size("sx")
    pipe_n = lax.axis_size("pipe")
    members = rows_n * cols_n
    head_total = head_class.shape[1]
    per_dev = head_total // members
    head_width = queries.shape[2] // head_total
    classes = head_class[0]
    blocks = kv_blocks[0]
    counts = kv_count[0]
    weight_local = out_weight[0]
    in_total, width_local = weight_local.shape
    in_rows = in_total // rows_n
    row_here = lax.axis_index("sy")
    col_here = lax.axis_index("sx")

    weight_pieces = [
        shifted(
            lax.dynamic_slice_in_dim(weight_local, ((row_here + step) % rows_n) * in_rows, in_rows, 0),
            "sy",
            step,
        )
        for step in range(rows_n)
    ]
    weight_mine = canonical(weight_pieces, row_here)

    tokens_here = queries.shape[1]
    pair_cols = per_dev * head_width

    def by_dest(tensor):
        return tensor[0].reshape(tokens_here, members, pair_cols).transpose(1, 0, 2)

    packed = jnp.concatenate([by_dest(queries), by_dest(keys), by_dest(values)], axis=2)
    exchanged = lax.all_to_all(packed, ("sy", "sx"), split_axis=0, concat_axis=0, tiled=True)
    token_total = tokens_here * members
    exchanged = exchanged.reshape(token_total, 3, per_dev, head_width)
    place = row_here * cols_n + col_here
    own_heads = place * per_dev + jnp.arange(per_dev, dtype=jnp.int32)
    joined = attend_dense(
        exchanged[:, 0],
        exchanged[:, 1],
        exchanged[:, 2],
        classes[own_heads] == 1,
        blocks[own_heads],
        counts[own_heads],
    )
    pair_rows = joined.shape[1]
    partial = None
    for step in range(cols_n):
        piece = shifted(joined, "sx", step)
        source = (col_here - step) % cols_n
        rows_w = lax.dynamic_slice_in_dim(weight_mine, source * pair_rows, pair_rows, 1)
        term = jnp.einsum(
            "te,kec->tkc", piece, rows_w, preferred_element_type=jnp.float32
        )
        partial = term if partial is None else partial + term
    token_total = partial.shape[0]
    chunk = token_total // rows_n
    partial = partial.reshape(token_total, rows_n * width_local).astype(jnp.bfloat16)
    reduced = None
    for step in range(rows_n):
        send = lax.dynamic_slice_in_dim(partial, ((row_here + step) % rows_n) * chunk, chunk, 0)
        got = shifted(send, "sy", step).astype(jnp.float32)
        reduced = got if reduced is None else reduced + got
    reduced = reduced.astype(jnp.bfloat16)
    rows_out = chunk // cols_n
    out_pieces = []
    for step in range(cols_n):
        send = lax.dynamic_slice_in_dim(reduced, ((col_here + step) % cols_n) * rows_out, rows_out, 0)
        pairs = [
            (p * cols_n + c, ((p + 1) % pipe_n) * cols_n + (c + step) % cols_n)
            for p in range(pipe_n)
            for c in range(cols_n)
        ]
        out_pieces.append(lax.ppermute(send, ("pipe", "sx"), pairs))
    ordered = canonical(out_pieces, col_here)
    handed = (
        ordered.reshape(cols_n, rows_out, rows_n, width_local)
        .transpose(1, 2, 0, 3)
        .reshape(rows_out, cols_n * rows_n * width_local)
    )
    return handed[None]


def solution(mesh):
    pipe_n, seq_n = mesh.devices.shape
    side = int(round(seq_n ** 0.5))
    grid = Mesh(mesh.devices.reshape(pipe_n, seq_n // side, side), ("pipe", "sy", "sx"))
    seq = ("sy", "sx")
    placed = (
        P("pipe", seq, None),
        P("pipe", seq, None),
        P("pipe", seq, None),
        P("pipe", None, seq),
        P("pipe", None),
        P("pipe", None, None, None),
        P("pipe", None),
    )
    return jax.shard_map(
        shards, mesh=grid, in_specs=placed, out_specs=P("pipe", seq, None), check_vma=False
    )
```

```python
import jax
import jax.numpy as jnp
from jax import lax
from jax.sharding import Mesh, PartitionSpec as P

FRAMES = 4
BLOCK = 64


def from_behind(value, axis, steps):
    count = lax.axis_size(axis)
    pairs = [(source, (source + steps) % count) for source in range(count)]
    return lax.ppermute(value, axis, pairs)


def frame_to_pos(tensor):
    token_total, row_width = tensor.shape
    return (
        tensor.reshape(FRAMES, token_total // FRAMES, row_width)
        .transpose(1, 0, 2)
        .reshape(token_total, row_width)
    )


def pos_to_frame(tensor):
    token_total, row_width = tensor.shape
    return (
        tensor.reshape(token_total // FRAMES, FRAMES, row_width)
        .transpose(1, 0, 2)
        .reshape(token_total, row_width)
    )


def block_of(temporal, token_total):
    tokens = jnp.arange(token_total, dtype=jnp.int32)
    per_frame = token_total // FRAMES
    spatial_block = tokens // BLOCK
    temporal_block = (tokens % per_frame) // (BLOCK // FRAMES)
    return jnp.where(temporal[:, None], temporal_block[None, :], spatial_block[None, :])


def attend_dense(query_rows, key_rows, value_rows, temporal, blocks, live_count):
    token_total, head_n, head_width = query_rows.shape
    nblock = token_total // BLOCK
    listed = jnp.arange(blocks.shape[-1], dtype=jnp.int32)
    live = listed[None, None, :] < live_count[:, None, None]
    chosen = (blocks[..., None] == jnp.arange(nblock, dtype=jnp.int32)) & live[..., None]
    allowed = jnp.any(chosen, axis=2).astype(jnp.bfloat16)
    owner = block_of(temporal, token_total)
    one_hot = (owner[..., None] == jnp.arange(nblock, dtype=jnp.int32)).astype(jnp.bfloat16)
    row_allowed = jnp.einsum("hqi,hib->hqb", one_hot, allowed, preferred_element_type=jnp.float32)
    keep = jnp.einsum(
        "hqb,hkb->hqk", row_allowed.astype(jnp.bfloat16), one_hot, preferred_element_type=jnp.float32
    )
    logit_scores = jnp.einsum(
        "qhd,khd->hqk", query_rows, key_rows, preferred_element_type=jnp.float32
    ) * (head_width ** (-0.5))
    logit_scores = jnp.where(keep > 0.5, logit_scores, -jnp.inf)
    row_max = jnp.max(logit_scores, axis=-1, keepdims=True)
    probs = jnp.exp(logit_scores - row_max)
    denom = jnp.sum(probs, axis=-1)
    weighted = jnp.einsum(
        "hqk,khd->qhd", probs.astype(jnp.bfloat16), value_rows, preferred_element_type=jnp.float32
    )
    result = weighted / jnp.transpose(denom)[..., None]
    return result.astype(jnp.bfloat16).reshape(token_total, head_n * head_width)


def shifted(value, axis, steps):
    count = lax.axis_size(axis)
    if steps % count == 0:
        return value
    pairs = [(source, (source + steps) % count) for source in range(count)]
    return lax.ppermute(value, axis, pairs)


def rows_at(tensor, index, size):
    return lax.dynamic_slice_in_dim(tensor, index * size, size, 0)


def roll_blocks(tensor, steps, blocks):
    rows_here, width = tensor.shape
    split = tensor.reshape(rows_here, blocks, width // blocks)
    return jnp.roll(split, steps, axis=1).reshape(rows_here, width)


def shards(queries, keys, values, out_weight, head_class, kv_blocks, kv_count):
    rows_n = lax.axis_size("sy")
    cols_n = lax.axis_size("sx")
    pipe_n = lax.axis_size("pipe")
    members = rows_n * cols_n
    head_total = head_class.shape[1]
    per_dev = head_total // members
    head_width = queries.shape[2] // head_total
    classes = head_class[0]
    blocks = kv_blocks[0]
    counts = kv_count[0]
    weight_local = out_weight[0]
    in_total, width_local = weight_local.shape
    in_rows = in_total // rows_n
    half_w = width_local // 2
    row_here = lax.axis_index("sy")
    col_here = lax.axis_index("sx")

    up_w = jnp.concatenate(
        [
            rows_at(weight_local, (row_here + 1) % rows_n, in_rows),
            rows_at(weight_local, (row_here + 2) % rows_n, in_rows)[:, :half_w],
        ],
        axis=1,
    )
    down_w = jnp.concatenate(
        [
            rows_at(weight_local, (row_here - 1) % rows_n, in_rows),
            rows_at(weight_local, (row_here + 2) % rows_n, in_rows)[:, half_w:],
        ],
        axis=1,
    )
    from_below = shifted(up_w, "sy", 1)
    from_above = shifted(down_w, "sy", -1)
    far_low = shifted(from_below[:, width_local:], "sy", 1)
    far_high = shifted(from_above[:, width_local:], "sy", -1)
    weight_rel = jnp.concatenate(
        [
            rows_at(weight_local, row_here, in_rows),
            from_below[:, :width_local],
            far_low,
            far_high,
            from_above[:, :width_local],
        ],
        axis=1,
    )

    tokens_here = queries.shape[1]
    pair_cols = per_dev * head_width

    def by_dest(tensor):
        return tensor[0].reshape(tokens_here, members, pair_cols).transpose(1, 0, 2)

    packed = jnp.concatenate([by_dest(queries), by_dest(keys), by_dest(values)], axis=2)
    exchanged = lax.all_to_all(packed, ("sy", "sx"), split_axis=0, concat_axis=0, tiled=True)
    token_total = tokens_here * members
    exchanged = exchanged.reshape(token_total, 3, per_dev, head_width)
    place = row_here * cols_n + col_here
    own_heads = place * per_dev + jnp.arange(per_dev, dtype=jnp.int32)
    joined = attend_dense(
        exchanged[:, 0],
        exchanged[:, 1],
        exchanged[:, 2],
        classes[own_heads] == 1,
        blocks[own_heads],
        counts[own_heads],
    )

    half_a = pair_cols // 2
    got_below = shifted(joined, "sx", 1)
    got_above = shifted(joined, "sx", -1)
    far_a = shifted(got_below[:, :half_a], "sx", 1)
    far_b = shifted(got_above[:, half_a:], "sx", -1)
    attended_pieces = (
        (joined, 0),
        (got_below, 1),
        (jnp.concatenate([far_a, far_b], axis=1), 2),
        (got_above, cols_n - 1),
    )
    partial = None
    for piece, step in attended_pieces:
        source = (col_here - step) % cols_n
        rows_w = rows_at(weight_rel, source, pair_cols)
        term = jnp.dot(piece, rows_w, preferred_element_type=jnp.float32)
        partial = term if partial is None else partial + term
    partial = partial.astype(jnp.bfloat16)

    chunk = token_total // rows_n
    half_c = chunk // 2
    far = rows_at(partial, (row_here + 2) % rows_n, chunk)
    far_up = roll_blocks(shifted(far[:half_c], "sy", 1), 1, rows_n).astype(jnp.float32)
    far_down = roll_blocks(shifted(far[half_c:], "sy", -1), -1, rows_n).astype(jnp.float32)
    next_up = rows_at(partial, (row_here + 1) % rows_n, chunk).astype(jnp.float32)
    next_up = jnp.concatenate([next_up[:half_c] + far_up, next_up[half_c:]], axis=0)
    next_down = rows_at(partial, (row_here - 1) % rows_n, chunk).astype(jnp.float32)
    next_down = jnp.concatenate([next_down[:half_c], next_down[half_c:] + far_down], axis=0)
    from_low = shifted(next_up.astype(jnp.bfloat16), "sy", 1)
    from_high = shifted(next_down.astype(jnp.bfloat16), "sy", -1)
    reduced = (
        rows_at(partial, row_here, chunk).astype(jnp.float32)
        + roll_blocks(from_low, 1, rows_n).astype(jnp.float32)
        + roll_blocks(from_high, -1, rows_n).astype(jnp.float32)
    ).astype(jnp.bfloat16)

    rows_out = chunk // cols_n
    out_pieces = []
    for step in range(cols_n):
        send = rows_at(reduced, (col_here + step) % cols_n, rows_out)
        pairs = [
            (p * cols_n + c, ((p + 1) % pipe_n) * cols_n + (c + step) % cols_n)
            for p in range(pipe_n)
            for c in range(cols_n)
        ]
        out_pieces.append(lax.ppermute(send, ("pipe", "sx"), pairs))
    stacked = jnp.stack(out_pieces).reshape(cols_n, rows_out, rows_n, width_local)
    src_row = jnp.arange(rows_n)[:, None]
    src_col = jnp.arange(cols_n)[None, :]
    pick_step = jnp.broadcast_to((col_here - src_col) % cols_n, (rows_n, cols_n))
    pick_block = jnp.broadcast_to((row_here - src_row) % rows_n, (rows_n, cols_n))
    chosen = stacked[pick_step, :, pick_block, :]
    handed = chosen.transpose(2, 0, 1, 3).reshape(rows_out, rows_n * cols_n * width_local)
    return handed[None]


def solution(mesh):
    pipe_n, seq_n = mesh.devices.shape
    side = int(round(seq_n ** 0.5))
    grid = Mesh(mesh.devices.reshape(pipe_n, seq_n // side, side), ("pipe", "sy", "sx"))
    seq = ("sy", "sx")
    placed = (
        P("pipe", seq, None),
        P("pipe", seq, None),
        P("pipe", seq, None),
        P("pipe", None, seq),
        P("pipe", None),
        P("pipe", None, None, None),
        P("pipe", None),
    )
    return jax.shard_map(
        shards, mesh=grid, in_specs=placed, out_specs=P("pipe", seq, None), check_vma=False
    )
```

```python
import jax
import jax.numpy as jnp
from jax import lax
from jax.sharding import Mesh, PartitionSpec as P

FRAMES = 4
BLOCK = 64


def from_behind(value, axis, steps):
    count = lax.axis_size(axis)
    pairs = [(source, (source + steps) % count) for source in range(count)]
    return lax.ppermute(value, axis, pairs)


def frame_to_pos(tensor):
    token_total, row_width = tensor.shape
    return (
        tensor.reshape(FRAMES, token_total // FRAMES, row_width)
        .transpose(1, 0, 2)
        .reshape(token_total, row_width)
    )


def pos_to_frame(tensor):
    token_total, row_width = tensor.shape
    return (
        tensor.reshape(token_total // FRAMES, FRAMES, row_width)
        .transpose(1, 0, 2)
        .reshape(token_total, row_width)
    )


def block_of(temporal, token_total):
    tokens = jnp.arange(token_total, dtype=jnp.int32)
    per_frame = token_total // FRAMES
    spatial_block = tokens // BLOCK
    temporal_block = (tokens % per_frame) // (BLOCK // FRAMES)
    return jnp.where(temporal[:, None], temporal_block[None, :], spatial_block[None, :])


def attend_dense(query_rows, key_rows, value_rows, temporal, blocks, live_count):
    token_total, head_n, head_width = query_rows.shape
    nblock = token_total // BLOCK
    listed = jnp.arange(blocks.shape[-1], dtype=jnp.int32)
    live = listed[None, None, :] < live_count[:, None, None]
    chosen = (blocks[..., None] == jnp.arange(nblock, dtype=jnp.int32)) & live[..., None]
    allowed = jnp.any(chosen, axis=2).astype(jnp.bfloat16)
    owner = block_of(temporal, token_total)
    one_hot = (owner[..., None] == jnp.arange(nblock, dtype=jnp.int32)).astype(jnp.bfloat16)
    row_allowed = jnp.einsum("hqi,hib->hqb", one_hot, allowed, preferred_element_type=jnp.float32)
    keep = jnp.einsum(
        "hqb,hkb->hqk", row_allowed.astype(jnp.bfloat16), one_hot, preferred_element_type=jnp.float32
    )
    logit_scores = jnp.einsum(
        "qhd,khd->hqk", query_rows, key_rows, preferred_element_type=jnp.float32
    ) * (head_width ** (-0.5))
    logit_scores = jnp.where(keep > 0.5, logit_scores, -jnp.inf)
    row_max = jnp.max(logit_scores, axis=-1, keepdims=True)
    probs = jnp.exp(logit_scores - row_max)
    denom = jnp.sum(probs, axis=-1)
    weighted = jnp.einsum(
        "hqk,khd->qhd", probs.astype(jnp.bfloat16), value_rows, preferred_element_type=jnp.float32
    )
    result = weighted / jnp.transpose(denom)[..., None]
    return result.astype(jnp.bfloat16).reshape(token_total, head_n * head_width)


def shifted(value, axis, steps):
    count = lax.axis_size(axis)
    if steps % count == 0:
        return value
    pairs = [(source, (source + steps) % count) for source in range(count)]
    return lax.ppermute(value, axis, pairs)


def rows_at(tensor, index, size):
    return lax.dynamic_slice_in_dim(tensor, index * size, size, 0)


def canonical(pieces, here):
    count = len(pieces)
    order = (here - jnp.arange(count)) % count
    return jnp.stack(pieces)[order]


def roll_blocks(tensor, steps, blocks):
    rows_here, width = tensor.shape
    split = tensor.reshape(rows_here, blocks, width // blocks)
    return jnp.roll(split, steps, axis=1).reshape(rows_here, width)


def shards(queries, keys, values, out_weight, head_class, kv_blocks, kv_count):
    rows_n = lax.axis_size("sy")
    cols_n = lax.axis_size("sx")
    pipe_n = lax.axis_size("pipe")
    members = rows_n * cols_n
    head_total = head_class.shape[1]
    per_dev = head_total // members
    head_width = queries.shape[2] // head_total
    classes = head_class[0]
    blocks = kv_blocks[0]
    counts = kv_count[0]
    weight_local = out_weight[0]
    in_total, width_local = weight_local.shape
    in_rows = in_total // rows_n
    half_w = width_local // 2
    row_here = lax.axis_index("sy")
    col_here = lax.axis_index("sx")

    up_w = jnp.concatenate(
        [
            rows_at(weight_local, (row_here + 1) % rows_n, in_rows),
            rows_at(weight_local, (row_here + 2) % rows_n, in_rows)[:, :half_w],
        ],
        axis=1,
    )
    down_w = jnp.concatenate(
        [
            rows_at(weight_local, (row_here - 1) % rows_n, in_rows),
            rows_at(weight_local, (row_here + 2) % rows_n, in_rows)[:, half_w:],
        ],
        axis=1,
    )
    from_below = shifted(up_w, "sy", 1)
    from_above = shifted(down_w, "sy", -1)
    tokens_here = queries.shape[1]
    pair_cols = per_dev * head_width

    def by_dest(tensor):
        return tensor[0].reshape(tokens_here, members, pair_cols).transpose(1, 0, 2)

    packed = jnp.concatenate([by_dest(queries), by_dest(keys), by_dest(values)], axis=2)
    exchanged = lax.all_to_all(packed, ("sy", "sx"), split_axis=0, concat_axis=0, tiled=True)
    token_total = tokens_here * members
    exchanged = exchanged.reshape(token_total, 3, per_dev, head_width)
    place = row_here * cols_n + col_here
    own_heads = place * per_dev + jnp.arange(per_dev, dtype=jnp.int32)
    joined = attend_dense(
        exchanged[:, 0],
        exchanged[:, 1],
        exchanged[:, 2],
        classes[own_heads] == 1,
        blocks[own_heads],
        counts[own_heads],
    )
    joined, from_below, from_above = lax.optimization_barrier((joined, from_below, from_above))
    far_low = shifted(from_below[:, width_local:], "sy", 1)
    far_high = shifted(from_above[:, width_local:], "sy", -1)
    weight_pieces = (
        (rows_at(weight_local, row_here, in_rows), 0),
        (from_below[:, :width_local], 1),
        (jnp.concatenate([far_low, far_high], axis=1), 2),
        (from_above[:, :width_local], rows_n - 1),
    )
    weight_mine = jnp.zeros((in_rows, rows_n * width_local), weight_local.dtype)
    for piece, step in weight_pieces:
        source = (row_here - step) % rows_n
        weight_mine = lax.dynamic_update_slice_in_dim(weight_mine, piece, source * width_local, 1)

    half_a = pair_cols // 2
    got_below = shifted(joined, "sx", 1)
    got_above = shifted(joined, "sx", -1)
    far_a = shifted(got_below[:, :half_a], "sx", 1)
    far_b = shifted(got_above[:, half_a:], "sx", -1)
    attended_pieces = (
        (joined, 0),
        (got_below, 1),
        (jnp.concatenate([far_a, far_b], axis=1), 2),
        (got_above, cols_n - 1),
    )
    partial = None
    for piece, step in attended_pieces:
        source = (col_here - step) % cols_n
        rows_w = rows_at(weight_mine, source, pair_cols)
        term = jnp.dot(piece, rows_w, preferred_element_type=jnp.float32)
        partial = term if partial is None else partial + term
    partial = partial.astype(jnp.bfloat16)

    chunk = token_total // rows_n
    reduced = None
    for step in range(rows_n):
        send = rows_at(partial, (row_here + step) % rows_n, chunk)
        got = shifted(send, "sy", step).astype(jnp.float32)
        reduced = got if reduced is None else reduced + got
    reduced = reduced.astype(jnp.bfloat16)
    rows_out = chunk // cols_n
    out_pieces = []
    for step in range(cols_n):
        send = rows_at(reduced, (col_here + step) % cols_n, rows_out)
        pairs = [
            (p * cols_n + c, ((p + 1) % pipe_n) * cols_n + (c + step) % cols_n)
            for p in range(pipe_n)
            for c in range(cols_n)
        ]
        out_pieces.append(lax.ppermute(send, ("pipe", "sx"), pairs))
    ordered = canonical(out_pieces, col_here)
    handed = (
        ordered.reshape(cols_n, rows_out, rows_n, width_local)
        .transpose(1, 2, 0, 3)
        .reshape(rows_out, cols_n * rows_n * width_local)
    )
    return handed[None]


def solution(mesh):
    pipe_n, seq_n = mesh.devices.shape
    side = int(round(seq_n ** 0.5))
    grid = Mesh(mesh.devices.reshape(pipe_n, seq_n // side, side), ("pipe", "sy", "sx"))
    seq = ("sy", "sx")
    placed = (
        P("pipe", seq, None),
        P("pipe", seq, None),
        P("pipe", seq, None),
        P("pipe", None, seq),
        P("pipe", None),
        P("pipe", None, None, None),
        P("pipe", None),
    )
    return jax.shard_map(
        shards, mesh=grid, in_specs=placed, out_specs=P("pipe", seq, None), check_vma=False
    )
```

```python
import jax
import jax.numpy as jnp
from jax import lax
from jax.sharding import Mesh, PartitionSpec as P

FRAMES = 4
BLOCK = 64


def from_behind(value, axis, steps):
    count = lax.axis_size(axis)
    pairs = [(source, (source + steps) % count) for source in range(count)]
    return lax.ppermute(value, axis, pairs)


def frame_to_pos(tensor):
    token_total, row_width = tensor.shape
    return (
        tensor.reshape(FRAMES, token_total // FRAMES, row_width)
        .transpose(1, 0, 2)
        .reshape(token_total, row_width)
    )


def pos_to_frame(tensor):
    token_total, row_width = tensor.shape
    return (
        tensor.reshape(token_total // FRAMES, FRAMES, row_width)
        .transpose(1, 0, 2)
        .reshape(token_total, row_width)
    )


def block_of(temporal, token_total):
    tokens = jnp.arange(token_total, dtype=jnp.int32)
    per_frame = token_total // FRAMES
    spatial_block = tokens // BLOCK
    temporal_block = (tokens % per_frame) // (BLOCK // FRAMES)
    return jnp.where(temporal[:, None], temporal_block[None, :], spatial_block[None, :])


def attend_dense(query_rows, key_rows, value_rows, temporal, blocks, live_count):
    token_total, head_n, head_width = query_rows.shape
    nblock = token_total // BLOCK
    listed = jnp.arange(blocks.shape[-1], dtype=jnp.int32)
    live = listed[None, None, :] < live_count[:, None, None]
    chosen = (blocks[..., None] == jnp.arange(nblock, dtype=jnp.int32)) & live[..., None]
    allowed = jnp.any(chosen, axis=2).astype(jnp.bfloat16)
    owner = block_of(temporal, token_total)
    one_hot = (owner[..., None] == jnp.arange(nblock, dtype=jnp.int32)).astype(jnp.bfloat16)
    row_allowed = jnp.einsum("hqi,hib->hqb", one_hot, allowed, preferred_element_type=jnp.float32)
    keep = jnp.einsum(
        "hqb,hkb->hqk", row_allowed.astype(jnp.bfloat16), one_hot, preferred_element_type=jnp.float32
    )
    logit_scores = jnp.einsum(
        "qhd,khd->hqk", query_rows, key_rows, preferred_element_type=jnp.float32
    ) * (head_width ** (-0.5))
    logit_scores = jnp.where(keep > 0.5, logit_scores, -jnp.inf)
    row_max = jnp.max(logit_scores, axis=-1, keepdims=True)
    probs = jnp.exp(logit_scores - row_max)
    denom = jnp.sum(probs, axis=-1)
    weighted = jnp.einsum(
        "hqk,khd->qhd", probs.astype(jnp.bfloat16), value_rows, preferred_element_type=jnp.float32
    )
    result = weighted / jnp.transpose(denom)[..., None]
    return result.astype(jnp.bfloat16).reshape(token_total, head_n * head_width)


def shifted(value, axis, steps):
    count = lax.axis_size(axis)
    if steps % count == 0:
        return value
    pairs = [(source, (source + steps) % count) for source in range(count)]
    return lax.ppermute(value, axis, pairs)


def rows_at(tensor, index, size):
    return lax.dynamic_slice_in_dim(tensor, index * size, size, 0)


def canonical(pieces, here):
    count = len(pieces)
    order = (here - jnp.arange(count)) % count
    return jnp.stack(pieces)[order]


def roll_blocks(tensor, steps, blocks):
    rows_here, width = tensor.shape
    split = tensor.reshape(rows_here, blocks, width // blocks)
    return jnp.roll(split, steps, axis=1).reshape(rows_here, width)


def shards(queries, keys, values, out_weight, head_class, kv_blocks, kv_count):
    rows_n = lax.axis_size("sy")
    cols_n = lax.axis_size("sx")
    pipe_n = lax.axis_size("pipe")
    members = rows_n * cols_n
    head_total = head_class.shape[1]
    per_dev = head_total // members
    head_width = queries.shape[2] // head_total
    classes = head_class[0]
    blocks = kv_blocks[0]
    counts = kv_count[0]
    weight_local = out_weight[0]
    in_total, width_local = weight_local.shape
    in_rows = in_total // rows_n
    half_w = width_local // 2
    row_here = lax.axis_index("sy")
    col_here = lax.axis_index("sx")

    up_w = jnp.concatenate(
        [
            rows_at(weight_local, (row_here + 1) % rows_n, in_rows),
            rows_at(weight_local, (row_here + 2) % rows_n, in_rows)[:, :half_w],
        ],
        axis=1,
    )
    down_w = jnp.concatenate(
        [
            rows_at(weight_local, (row_here - 1) % rows_n, in_rows),
            rows_at(weight_local, (row_here + 2) % rows_n, in_rows)[:, half_w:],
        ],
        axis=1,
    )
    from_below = shifted(up_w, "sy", 1)
    from_above = shifted(down_w, "sy", -1)
    tokens_here = queries.shape[1]
    pair_cols = per_dev * head_width

    def by_dest(tensor):
        return tensor[0].reshape(tokens_here, members, pair_cols).transpose(1, 0, 2)

    packed = jnp.concatenate([by_dest(queries), by_dest(keys), by_dest(values)], axis=2)
    exchanged = lax.all_to_all(packed, ("sy", "sx"), split_axis=0, concat_axis=0, tiled=True)
    token_total = tokens_here * members
    exchanged = exchanged.reshape(token_total, 3, per_dev, head_width)
    place = row_here * cols_n + col_here
    own_heads = place * per_dev + jnp.arange(per_dev, dtype=jnp.int32)
    joined = attend_dense(
        exchanged[:, 0],
        exchanged[:, 1],
        exchanged[:, 2],
        classes[own_heads] == 1,
        blocks[own_heads],
        counts[own_heads],
    )
    joined, from_below, from_above = lax.optimization_barrier((joined, from_below, from_above))
    far_low = shifted(from_below[:, width_local:], "sy", 1)
    far_high = shifted(from_above[:, width_local:], "sy", -1)
    weight_pieces = (
        (rows_at(weight_local, row_here, in_rows), 0),
        (from_below[:, :width_local], 1),
        (jnp.concatenate([far_low, far_high], axis=1), 2),
        (from_above[:, :width_local], rows_n - 1),
    )
    weight_mine = jnp.zeros((in_rows, rows_n * width_local), weight_local.dtype)
    for piece, step in weight_pieces:
        source = (row_here - step) % rows_n
        weight_mine = lax.dynamic_update_slice_in_dim(weight_mine, piece, source * width_local, 1)

    half_a = pair_cols // 2
    got_below = shifted(joined, "sx", 1)
    got_above = shifted(joined, "sx", -1)
    far_a = shifted(got_below[:, :half_a], "sx", 1)
    far_b = shifted(got_above[:, half_a:], "sx", -1)
    attended_pieces = (
        (joined, 0),
        (got_below, 1),
        (jnp.concatenate([far_a, far_b], axis=1), 2),
        (got_above, cols_n - 1),
    )
    partial = None
    for piece, step in attended_pieces:
        source = (col_here - step) % cols_n
        rows_w = rows_at(weight_mine, source, pair_cols)
        term = jnp.dot(piece, rows_w, preferred_element_type=jnp.float32)
        partial = term if partial is None else partial + term
    chunk = token_total // rows_n
    half_c = chunk // 2
    far = rows_at(partial, (row_here + 2) % rows_n, chunk).astype(jnp.bfloat16)
    far_up = shifted(far[:half_c], "sy", 1).astype(jnp.float32)
    far_down = shifted(far[half_c:], "sy", -1).astype(jnp.float32)
    next_up = rows_at(partial, (row_here + 1) % rows_n, chunk)
    next_up = next_up.at[:half_c].add(far_up)
    next_down = rows_at(partial, (row_here - 1) % rows_n, chunk)
    next_down = next_down.at[half_c:].add(far_down)
    from_low = shifted(next_up.astype(jnp.bfloat16), "sy", 1)
    from_high = shifted(next_down.astype(jnp.bfloat16), "sy", -1)
    reduced = (
        rows_at(partial, row_here, chunk)
        + from_low.astype(jnp.float32)
        + from_high.astype(jnp.float32)
    ).astype(jnp.bfloat16)
    rows_out = chunk // cols_n
    out_pieces = []
    for step in range(cols_n):
        send = rows_at(reduced, (col_here + step) % cols_n, rows_out)
        pairs = [
            (p * cols_n + c, ((p + 1) % pipe_n) * cols_n + (c + step) % cols_n)
            for p in range(pipe_n)
            for c in range(cols_n)
        ]
        out_pieces.append(lax.ppermute(send, ("pipe", "sx"), pairs))
    ordered = canonical(out_pieces, col_here)
    handed = (
        ordered.reshape(cols_n, rows_out, rows_n, width_local)
        .transpose(1, 2, 0, 3)
        .reshape(rows_out, cols_n * rows_n * width_local)
    )
    return handed[None]


def solution(mesh):
    pipe_n, seq_n = mesh.devices.shape
    side = int(round(seq_n ** 0.5))
    grid = Mesh(mesh.devices.reshape(pipe_n, seq_n // side, side), ("pipe", "sy", "sx"))
    seq = ("sy", "sx")
    placed = (
        P("pipe", seq, None),
        P("pipe", seq, None),
        P("pipe", seq, None),
        P("pipe", None, seq),
        P("pipe", None),
        P("pipe", None, None, None),
        P("pipe", None),
    )
    return jax.shard_map(
        shards, mesh=grid, in_specs=placed, out_specs=P("pipe", seq, None), check_vma=False
    )
```
